256 devices in a mesh: blk: 128 (over z, x, y_hi, core), pair: 2 (over y_lo).
Axes of the slice: x: 4, y: 4 (y_hi: 2, y_lo: 2; y = y_hi * 2 + y_lo), z: 8, core: 2. Of those that a mesh axis runs over, the one named last changes fastest.
Arguments:
- images: bfloat16 [114688, 768], P(('blk', 'pair')), may hold values from -1 to 1
- texts: bfloat16 [114688, 768], P(('blk', 'pair')), may hold values from -1 to 1
- scale: float32 [], replicated, may hold values from 4 to 16
- bias: float32 [], replicated, may hold values from -6 to -2
Outputs:
- row_loss: float32 [114688], P(('blk', 'pair'))
- grad_images: float32 [114688, 768], P(('blk', 'pair'))
- grad_texts: float32 [114688, 768], P(('blk', 'pair'))
The draws below stay inside these ranges and needn't reach their ends.
All inputs are finite; a program needn't handle non-finite values.
Results may differ from the reference program's by a relative error of at most 0.0056.
Values may be sent and summed in bfloat16 or wider, within the bound.
No kernel may reach another device: no remote copies, remote signals or barrier semaphores. Data moves between devices by JAX's collectives and lax.ppermute only.
A program may use at most 128 MiB of HBM per device.

```python
import math
import jax
import jax.numpy as jnp
from jax import lax

D = 768
ROWS = 448
STEPS = 6
PAIRS = 114688
N_BLK = 128
N_PAIR = 2


def feature_pair(key):
    subkeys = [jax.random.fold_in(key, 11 + c) for c in range(7)]
    extent = (PAIRS, D)
    shared = jax.random.normal(subkeys[0], extent, jnp.float32)
    noise_picture = jax.random.normal(subkeys[1], extent, jnp.float32)
    noise_caption = jax.random.normal(subkeys[2], extent, jnp.float32)
    columns = jnp.exp(jax.random.uniform(subkeys[3], (1, D), jnp.float32, 0.0, math.log(10.0)))
    rows_picture = jnp.exp(jax.random.uniform(subkeys[4], (PAIRS, 1), jnp.float32, 0.0, math.log(10.0)))
    rows_caption = jnp.exp(jax.random.uniform(subkeys[5], (PAIRS, 1), jnp.float32, 0.0, math.log(10.0)))
    picture = jnp.clip((shared + 0.5 * noise_picture) * columns * rows_picture * 0.004, -1.0, 1.0)
    caption = jnp.clip((0.8 * shared + 0.6 * noise_caption) * columns * rows_caption * 0.004, -1.0, 1.0)
    return (picture, caption)


def draw_images(key, part):
    return feature_pair(key)[0].astype(jnp.bfloat16)


def draw_texts(key, part):
    return feature_pair(key)[1].astype(jnp.bfloat16)


def setup_inputs(seed: int = 0) -> dict:
    arg_keys = jax.random.split(jax.random.key(seed), 5)
    return {
        "images": draw_images(jax.random.fold_in(arg_keys[4], 71), 0),
        "texts": draw_texts(jax.random.fold_in(arg_keys[4], 71), 0),
        "scale": jnp.clip(jnp.exp(jax.random.uniform(arg_keys[2], (), jnp.float32, math.log(4.0), math.log(16.0))), 4.0, 16.0),
        "bias": jnp.clip(jax.random.uniform(arg_keys[3], (), jnp.float32, -6.0, -2.0), -6.0, -2.0),
    }


EPSILON = 1e-06

def unit_rows(features):
    widened = features.astype(jnp.float32)
    inverse = lax.rsqrt(lax.optimization_barrier(jnp.sum(widened * widened, axis=1, keepdims=True)) + EPSILON)
    return (widened * inverse, inverse)

def tangent(unit, inverse, direction):
    return inverse * (direction - unit * lax.optimization_barrier(jnp.sum(unit * direction, axis=1, keepdims=True)))

def reference(images, texts, scale, bias):
    group = N_PAIR * ROWS
    image_unit, image_inverse = unit_rows(images)
    text_unit, text_inverse = unit_rows(texts)
    image_groups = image_unit.astype(jnp.bfloat16).reshape(N_BLK, group, D)
    text_groups = text_unit.astype(jnp.bfloat16).reshape(N_BLK, group, D)
    diagonal = lax.broadcasted_iota(jnp.int32, (group, group), 0) == lax.broadcasted_iota(jnp.int32, (group, group), 1)
    loss_total = jnp.zeros((N_BLK, group), jnp.float32)
    image_dir = jnp.zeros((N_BLK, group, D), jnp.float32)
    text_dir = jnp.zeros((N_BLK, group, D), jnp.float32)
    for offset in range(STEPS):
        shifted = jnp.roll(text_groups, offset, axis=0)
        if offset == 0:
            labels = jnp.where(diagonal, 1.0, -1.0).astype(jnp.float32)
        else:
            labels = jnp.full((group, group), -1.0, jnp.float32)

        def visit_group(operands, labels=labels):
            image_block, text_block = operands
            logits = scale * jnp.dot(image_block, text_block.T, preferred_element_type=jnp.float32) + bias
            margin = labels * logits
            loss_rows = lax.optimization_barrier(jnp.sum(jax.nn.softplus(-margin), axis=1))
            weights_bf = (scale * -labels * jax.nn.sigmoid(-margin)).astype(jnp.bfloat16)
            image_grad = jnp.dot(weights_bf, text_block, preferred_element_type=jnp.float32)
            text_grad = jnp.dot(weights_bf.T, image_block, preferred_element_type=jnp.float32)
            return (loss_rows, image_grad, text_grad)
        loss_rows, image_grad, text_grad = lax.map(visit_group, (image_groups, shifted))
        loss_total = loss_total + loss_rows
        image_dir = image_dir + image_grad
        text_dir = text_dir + jnp.roll(text_grad, -offset, axis=0)
    row_loss = loss_total.reshape(PAIRS) / (STEPS * group)
    grad_images = tangent(image_unit, image_inverse, image_dir.reshape(PAIRS, D))
    grad_texts = tangent(text_unit, text_inverse, text_dir.reshape(PAIRS, D))
    return (row_loss, grad_images, grad_texts)
```

```python
import jax
import jax.numpy as jnp
import numpy as np
from jax import lax
from jax.sharding import PartitionSpec as P

STEPS = 6


EPSILON = 1e-06


def unit_rows(features):
    widened = features.astype(jnp.float32)
    inverse = lax.rsqrt(jnp.sum(widened * widened, axis=1, keepdims=True) + EPSILON)
    return (widened * inverse, inverse)


def tangent(unit, inverse, direction):
    return inverse * (direction - unit * jnp.sum(unit * direction, axis=1, keepdims=True))


def device_coords(mesh):
    try:
        devices = mesh.devices
        return np.array([[d.coords for d in row] for row in devices])
    except Exception:
        return None


def hops(coords, shape, a, b):
    if coords is None:
        return 0
    delta = np.abs(coords[a] - coords[b])
    return int(np.sum(np.minimum(delta, np.array(shape) - delta)))


def group_routes(mesh, shift):
    n_blk, n_pair = mesh.shape["blk"], mesh.shape["pair"]
    coords = device_coords(mesh)
    shape = None
    if coords is not None:
        shape = tuple(int(v) + 1 for v in coords.reshape(-1, 3).max(axis=0))
    route = []
    for g in range(n_blk):
        h = (g + shift) % n_blk
        same = sum(hops(coords, shape, (g, p), (h, p)) for p in range(n_pair))
        cross = sum(hops(coords, shape, (g, p), (h, n_pair - 1 - p)) for p in range(n_pair))
        for p in range(n_pair):
            q = p if same <= cross else n_pair - 1 - p
            route.append((g * n_pair + p, h * n_pair + q))
    return route


def score(mine, block, diagonal, scale, bias):
    logits = (
        scale
        * lax.dot_general(
            mine, block, (((1,), (1,)), ((), ())), preferred_element_type=jnp.float32
        )
        + bias
    )
    if diagonal:
        column = lax.broadcasted_iota(jnp.int32, logits.shape, 1)
        target = lax.broadcasted_iota(jnp.int32, logits.shape, 0) + lax.axis_index("pair") * mine.shape[0]
        labels = jnp.where(column == target, 1.0, -1.0).astype(jnp.float32)
    else:
        labels = -1.0
    margin = labels * logits
    weights_bf = (scale * -labels * jax.nn.sigmoid(-margin)).astype(jnp.bfloat16)
    return margin, weights_bf


def make_body(mesh):
    pair_route = [(i, i ^ 1) for i in range(mesh.shape["blk"] * mesh.shape["pair"])]
    text_routes = [group_routes(mesh, k) for k in range(1, STEPS)]
    image_routes = [group_routes(mesh, -k) for k in range(1, STEPS)]
    axes = ("blk", "pair")

    def body(images, texts, scale, bias):
        rows = images.shape[0]
        image_unit, image_inverse = unit_rows(images)
        text_unit, text_inverse = unit_rows(texts)
        image_emb = image_unit.astype(jnp.bfloat16)
        text_emb = text_unit.astype(jnp.bfloat16)
        mine = jnp.concatenate([text_emb, image_emb], axis=0)
        other = lax.ppermute(mine, axes, pair_route)
        first = lax.axis_index("pair") == 0
        text_group = jnp.where(first, jnp.concatenate([text_emb, other[:rows]], 0),
                               jnp.concatenate([other[:rows], text_emb], 0))
        image_group = jnp.where(first, jnp.concatenate([image_emb, other[rows:]], 0),
                                jnp.concatenate([other[rows:], image_emb], 0))
        text_blocks = [text_group] + [lax.ppermute(text_group, axes, r) for r in text_routes]
        image_blocks = [image_group] + [lax.ppermute(image_group, axes, r) for r in image_routes]
        loss_total = jnp.zeros((rows,), jnp.float32)
        image_dir = jnp.zeros(images.shape, jnp.float32)
        text_dir = jnp.zeros(texts.shape, jnp.float32)
        for offset in range(STEPS):
            margin, weights = score(image_emb, text_blocks[offset], offset == 0, scale, bias)
            loss_total = loss_total + jnp.sum(jax.nn.softplus(-margin), axis=1)
            image_dir = image_dir + jnp.dot(weights, text_blocks[offset], preferred_element_type=jnp.float32)
            _, weights_t = score(text_emb, image_blocks[offset], offset == 0, scale, bias)
            text_dir = text_dir + jnp.dot(weights_t, image_blocks[offset], preferred_element_type=jnp.float32)
        window = STEPS * lax.axis_size("pair") * rows
        row_loss = loss_total / window
        grad_images = tangent(image_unit, image_inverse, image_dir)
        grad_texts = tangent(text_unit, text_inverse, text_dir)
        return (row_loss, grad_images, grad_texts)

    return body


def solution(mesh):
    in_specs = (P(("blk", "pair"), None), P(("blk", "pair"), None), P(), P())
    out_specs = (P(("blk", "pair")), P(("blk", "pair"), None), P(("blk", "pair"), None))
    return jax.shard_map(make_body(mesh), mesh=mesh, in_specs=in_specs, out_specs=out_specs, check_vma=False)
```

```python
import jax
import jax.numpy as jnp
from jax import lax
from jax.sharding import PartitionSpec as P

STEPS = 6


EPSILON = 1e-06


def unit_rows(features):
    widened = features.astype(jnp.float32)
    inverse = lax.rsqrt(jnp.sum(widened * widened, axis=1, keepdims=True) + EPSILON)
    return (widened * inverse, inverse)


def tangent(unit, inverse, direction):
    return inverse * (direction - unit * jnp.sum(unit * direction, axis=1, keepdims=True))


def score(mine, block, diagonal, scale, bias):
    logits = (
        scale
        * lax.dot_general(
            mine, block, (((1,), (1,)), ((), ())), preferred_element_type=jnp.float32
        )
        + bias
    )
    if diagonal:
        column = lax.broadcasted_iota(jnp.int32, logits.shape, 1)
        row = lax.broadcasted_iota(jnp.int32, logits.shape, 0)
        labels = jnp.where(column == row, 1.0, -1.0).astype(jnp.float32)
    else:
        labels = -1.0
    margin = labels * logits
    weights_bf = (scale * -labels * jax.nn.sigmoid(-margin)).astype(jnp.bfloat16)
    return margin, weights_bf


def make_body(mesh):
    n_blk, n_pair = mesh.shape["blk"], mesh.shape["pair"]
    pair_route = [(i, i ^ 1) for i in range(n_blk * n_pair)]

    def shifted(shift, flip):
        return [(g * n_pair + p, ((g + shift) % n_blk) * n_pair + (p ^ flip))
                for g in range(n_blk) for p in range(n_pair)]

    axes = ("blk", "pair")

    def body(images, texts, scale, bias):
        rows = images.shape[0]
        image_unit, image_inverse = unit_rows(images)
        text_unit, text_inverse = unit_rows(texts)
        image_emb = image_unit.astype(jnp.bfloat16)
        text_emb = text_unit.astype(jnp.bfloat16)
        other = lax.ppermute(jnp.concatenate([text_emb, image_emb], axis=0), axes, pair_route)
        text_blocks = [(text_emb, True), (other[:rows], False)]
        image_blocks = [(image_emb, True), (other[rows:], False)]
        for offset in range(1, STEPS):
            for flip in range(n_pair):
                text_blocks.append((lax.ppermute(text_emb, axes, shifted(offset, flip)), False))
                image_blocks.append((lax.ppermute(image_emb, axes, shifted(-offset, flip)), False))
        loss_total = jnp.zeros((rows,), jnp.float32)
        image_dir = jnp.zeros(images.shape, jnp.float32)
        text_dir = jnp.zeros(texts.shape, jnp.float32)
        for (text_block, diagonal), (image_block, _) in zip(text_blocks, image_blocks):
            margin, weights = score(image_emb, text_block, diagonal, scale, bias)
            loss_total = loss_total + jnp.sum(jax.nn.softplus(-margin), axis=1)
            image_dir = image_dir + jnp.dot(weights, text_block, preferred_element_type=jnp.float32)
            _, weights_t = score(text_emb, image_block, diagonal, scale, bias)
            text_dir = text_dir + jnp.dot(weights_t, image_block, preferred_element_type=jnp.float32)
        window = STEPS * n_pair * rows
        row_loss = loss_total / window
        grad_images = tangent(image_unit, image_inverse, image_dir)
        grad_texts = tangent(text_unit, text_inverse, text_dir)
        return (row_loss, grad_images, grad_texts)

    return body


def solution(mesh):
    in_specs = (P(("blk", "pair"), None), P(("blk", "pair"), None), P(), P())
    out_specs = (P(("blk", "pair")), P(("blk", "pair"), None), P(("blk", "pair"), None))
    return jax.shard_map(make_body(mesh), mesh=mesh, in_specs=in_specs, out_specs=out_specs, check_vma=False)
```

```python
import jax
import jax.numpy as jnp
import numpy as np
from jax import lax
from jax.sharding import PartitionSpec as P

STEPS = 6


EPSILON = 1e-06


def unit_rows(features):
    widened = features.astype(jnp.float32)
    inverse = lax.rsqrt(jnp.sum(widened * widened, axis=1, keepdims=True) + EPSILON)
    return (widened * inverse, inverse)


def tangent(unit, inverse, direction):
    return inverse * (direction - unit * jnp.sum(unit * direction, axis=1, keepdims=True))


def score(mine, block, diagonal, scale, bias):
    logits = (
        scale
        * lax.dot_general(
            mine, block, (((1,), (1,)), ((), ())), preferred_element_type=jnp.float32
        )
        + bias
    )
    if diagonal:
        column = lax.broadcasted_iota(jnp.int32, logits.shape, 1)
        target = lax.broadcasted_iota(jnp.int32, logits.shape, 0) + lax.axis_index("pair") * mine.shape[0]
        labels = jnp.where(column == target, 1.0, -1.0).astype(jnp.float32)
    else:
        labels = -1.0
    margin = labels * logits
    weights_bf = (scale * -labels * jax.nn.sigmoid(-margin)).astype(jnp.bfloat16)
    return margin, weights_bf


def chip_coords(mesh):
    try:
        return np.array([[d.coords for d in row] for row in mesh.devices])
    except Exception:
        return None


def block_route(mesh, coords, send):
    n_blk, n_pair = mesh.shape["blk"], mesh.shape["pair"]
    torus = None if coords is None else coords.reshape(-1, 3).max(axis=0) + 1

    def hops(a, b):
        if coords is None:
            return 0
        delta = np.abs(coords[a] - coords[b])
        return int(np.sum(np.minimum(delta, torus - delta)))

    route = []
    for g in range(n_blk):
        h = send(g) % n_blk
        same = sum(hops((g, p), (h, p)) for p in range(n_pair))
        cross = sum(hops((g, p), (h, n_pair - 1 - p)) for p in range(n_pair))
        for p in range(n_pair):
            q = p if same <= cross else n_pair - 1 - p
            route.append((g * n_pair + p, h * n_pair + q))
    return route


def make_body(mesh):
    n_blk, n_pair = mesh.shape["blk"], mesh.shape["pair"]
    coords = chip_coords(mesh)
    axes = ("blk", "pair")
    pair_route = [(i, i ^ 1) for i in range(n_blk * n_pair)]
    core_route = [(g * n_pair + p, (g ^ 1) * n_pair + p) for g in range(n_blk) for p in range(n_pair)]
    route_a = block_route(mesh, coords, lambda g: g + (4 if g % 2 == 0 else 2))
    route_b = block_route(mesh, coords, lambda g: g + (-2 if g % 2 == 0 else -4))
    route_c = block_route(mesh, coords, lambda g: g + (3 if g % 2 == 0 else 5))
    route_d = block_route(mesh, coords, lambda g: g + (-3 if g % 2 == 0 else 3))
    route_f = block_route(mesh, coords, lambda g: g + (-5 if g % 2 == 0 else -3))

    def body(images, texts, scale, bias):
        rows = images.shape[0]
        image_unit, image_inverse = unit_rows(images)
        text_unit, text_inverse = unit_rows(texts)
        image_emb = image_unit.astype(jnp.bfloat16)
        text_emb = text_unit.astype(jnp.bfloat16)
        other = lax.ppermute(jnp.concatenate([text_emb, image_emb], axis=0), axes, pair_route)
        first = lax.axis_index("pair") == 0
        even = lax.axis_index("blk") % 2 == 0
        text_group = jnp.where(first, jnp.concatenate([text_emb, other[:rows]], 0),
                               jnp.concatenate([other[:rows], text_emb], 0))
        image_group = jnp.where(first, jnp.concatenate([image_emb, other[rows:]], 0),
                                jnp.concatenate([other[rows:], image_emb], 0))

        def send(block, route):
            return lax.ppermute(block, axes, route)

        got_a = send(text_group, route_a)
        got_b = send(image_group, route_b)
        got_c = send(text_group, route_c)
        got_d = send(jnp.where(even, image_group, text_group), route_d)
        got_f = send(image_group, route_f)
        swap_own = send(jnp.where(even, text_group, image_group), core_route)
        swap_a = send(got_a, core_route)
        swap_b = send(got_b, core_route)
        swap_d = send(got_d, core_route)
        swap_cf = send(jnp.where(even, got_f, got_c), core_route)
        text_blocks = [got_a, got_c, swap_a,
                       jnp.where(even, got_d, swap_d), jnp.where(even, swap_cf, swap_own)]
        image_blocks = [got_b, got_f, swap_b,
                        jnp.where(even, swap_d, got_d), jnp.where(even, swap_own, swap_cf)]
        loss_total = jnp.zeros((rows,), jnp.float32)
        image_dir = jnp.zeros(images.shape, jnp.float32)
        text_dir = jnp.zeros(texts.shape, jnp.float32)
        visits = [(text_group, image_group, True)] + [
            (t, i, False) for t, i in zip(text_blocks, image_blocks)]
        for text_block, image_block, diagonal in visits:
            margin, weights = score(image_emb, text_block, diagonal, scale, bias)
            loss_total = loss_total + jnp.sum(jax.nn.softplus(-margin), axis=1)
            image_dir = image_dir + jnp.dot(weights, text_block, preferred_element_type=jnp.float32)
            _, weights_t = score(text_emb, image_block, diagonal, scale, bias)
            text_dir = text_dir + jnp.dot(weights_t, image_block, preferred_element_type=jnp.float32)
        window = STEPS * n_pair * rows
        row_loss = loss_total / window
        grad_images = tangent(image_unit, image_inverse, image_dir)
        grad_texts = tangent(text_unit, text_inverse, text_dir)
        return (row_loss, grad_images, grad_texts)

    return body


def solution(mesh):
    in_specs = (P(("blk", "pair"), None), P(("blk", "pair"), None), P(), P())
    out_specs = (P(("blk", "pair")), P(("blk", "pair"), None), P(("blk", "pair"), None))
    return jax.shard_map(make_body(mesh), mesh=mesh, in_specs=in_specs, out_specs=out_specs, check_vma=False)
```

```python
import jax
import jax.numpy as jnp
import numpy as np
from jax import lax
from jax.experimental import pallas as pl
from jax.experimental.pallas import tpu as pltpu
from jax.sharding import PartitionSpec as P

STEPS = 6


EPSILON = 1e-06


def unit_rows(features):
    widened = features.astype(jnp.float32)
    inverse = lax.rsqrt(jnp.sum(widened * widened, axis=1, keepdims=True) + EPSILON)
    return (widened * inverse, inverse)


def tangent(unit, inverse, direction):
    return inverse * (direction - unit * jnp.sum(unit * direction, axis=1, keepdims=True))


def score(mine, block, diagonal, scale, bias):
    logits = (
        scale
        * lax.dot_general(
            mine, block, (((1,), (1,)), ((), ())), preferred_element_type=jnp.float32
        )
        + bias
    )
    if diagonal:
        column = lax.broadcasted_iota(jnp.int32, logits.shape, 1)
        target = lax.broadcasted_iota(jnp.int32, logits.shape, 0) + lax.axis_index("pair") * mine.shape[0]
        labels = jnp.where(column == target, 1.0, -1.0).astype(jnp.float32)
    else:
        labels = -1.0
    margin = labels * logits
    weights_bf = (scale * -labels * jax.nn.sigmoid(-margin)).astype(jnp.bfloat16)
    return margin, weights_bf


def chip_coords(mesh):
    try:
        return np.array([[d.coords for d in row] for row in mesh.devices])
    except Exception:
        return None


def block_route(mesh, coords, send):
    n_blk, n_pair = mesh.shape["blk"], mesh.shape["pair"]
    torus = None if coords is None else coords.reshape(-1, 3).max(axis=0) + 1

    def hops(a, b):
        if coords is None:
            return 0
        delta = np.abs(coords[a] - coords[b])
        return int(np.sum(np.minimum(delta, torus - delta)))

    route = []
    for g in range(n_blk):
        h = send(g) % n_blk
        same = sum(hops((g, p), (h, p)) for p in range(n_pair))
        cross = sum(hops((g, p), (h, n_pair - 1 - p)) for p in range(n_pair))
        for p in range(n_pair):
            q = p if same <= cross else n_pair - 1 - p
            route.append((g * n_pair + p, h * n_pair + q))
    return route


def visit_kernel(diagonal, with_loss):
    def kernel(params_ref, offset_ref, mine_ref, block_ref, dir_in_ref, loss_in_ref, dir_ref, loss_ref):
        scale = params_ref[0]
        bias = params_ref[1]
        block = block_ref[...]
        logits = scale * lax.dot_general(
            mine_ref[...], block, (((1,), (1,)), ((), ())), preferred_element_type=jnp.float32
        ) + bias
        if diagonal:
            column = lax.broadcasted_iota(jnp.int32, logits.shape, 1)
            row = lax.broadcasted_iota(jnp.int32, logits.shape, 0) + offset_ref[0]
            positive = column == row
            margin = jnp.where(positive, logits, -logits)
            factor = jnp.where(positive, -scale, scale)
        else:
            margin = -logits
            factor = scale
        small = jnp.exp(-jnp.abs(margin))
        if with_loss:
            terms = jnp.maximum(-margin, 0.0) + jnp.log1p(small)
            loss_ref[...] = loss_in_ref[...] + jnp.sum(terms, axis=1, keepdims=True)
        else:
            loss_ref[...] = loss_in_ref[...]
        sigmoid = jnp.where(margin >= 0, small, 1.0) / (1.0 + small)
        weights = (factor * sigmoid).astype(jnp.bfloat16)
        dir_ref[...] = dir_in_ref[...] + jnp.dot(weights, block, preferred_element_type=jnp.float32)

    return kernel


def visit(mine, block, direction, loss, params, offset, diagonal, with_loss):
    rows = mine.shape[0]
    smem = pl.BlockSpec(memory_space=pltpu.SMEM)
    vmem = pl.BlockSpec(memory_space=pltpu.VMEM)
    return pl.pallas_call(
        visit_kernel(diagonal, with_loss),
        out_shape=(jax.ShapeDtypeStruct(direction.shape, jnp.float32),
                   jax.ShapeDtypeStruct((rows, 1), jnp.float32)),
        in_specs=[smem, smem, vmem, vmem, vmem, vmem],
        out_specs=(vmem, vmem),
        input_output_aliases={4: 0, 5: 1},
    )(params, offset, mine, block, direction, loss)


def make_body(mesh):
    n_blk, n_pair = mesh.shape["blk"], mesh.shape["pair"]
    coords = chip_coords(mesh)
    axes = ("blk", "pair")
    pair_route = [(i, i ^ 1) for i in range(n_blk * n_pair)]
    core_route = [(g * n_pair + p, (g ^ 1) * n_pair + p) for g in range(n_blk) for p in range(n_pair)]
    route_a = block_route(mesh, coords, lambda g: g + (4 if g % 2 == 0 else 2))
    route_b = block_route(mesh, coords, lambda g: g + (-2 if g % 2 == 0 else -4))
    route_c = block_route(mesh, coords, lambda g: g + (3 if g % 2 == 0 else 5))
    route_d = block_route(mesh, coords, lambda g: g + (-3 if g % 2 == 0 else 3))
    route_f = block_route(mesh, coords, lambda g: g + (-5 if g % 2 == 0 else -3))

    def body(images, texts, scale, bias):
        rows = images.shape[0]
        image_unit, image_inverse = unit_rows(images)
        text_unit, text_inverse = unit_rows(texts)
        image_emb = image_unit.astype(jnp.bfloat16)
        text_emb = text_unit.astype(jnp.bfloat16)
        other = lax.ppermute(jnp.concatenate([text_emb, image_emb], axis=0), axes, pair_route)
        first = lax.axis_index("pair") == 0
        even = lax.axis_index("blk") % 2 == 0
        text_group = jnp.where(first, jnp.concatenate([text_emb, other[:rows]], 0),
                               jnp.concatenate([other[:rows], text_emb], 0))
        image_group = jnp.where(first, jnp.concatenate([image_emb, other[rows:]], 0),
                                jnp.concatenate([other[rows:], image_emb], 0))

        def send(block, route):
            return lax.ppermute(block, axes, route)

        got_a = send(text_group, route_a)
        got_b = send(image_group, route_b)
        got_c = send(text_group, route_c)
        got_d = send(jnp.where(even, image_group, text_group), route_d)
        got_f = send(image_group, route_f)
        swap_own = send(jnp.where(even, text_group, image_group), core_route)
        swap_a = send(got_a, core_route)
        swap_b = send(got_b, core_route)
        swap_d = send(got_d, core_route)
        swap_cf = send(jnp.where(even, got_f, got_c), core_route)
        text_blocks = [got_a, got_c, swap_a,
                       jnp.where(even, got_d, swap_d), jnp.where(even, swap_cf, swap_own)]
        image_blocks = [got_b, got_f, swap_b,
                        jnp.where(even, swap_d, got_d), jnp.where(even, swap_own, swap_cf)]
        params = jnp.stack([scale, bias]).astype(jnp.float32)
        offset = (lax.axis_index("pair") * rows).astype(jnp.int32).reshape(1)
        loss_total = jnp.zeros((rows, 1), jnp.float32)
        unused = jnp.zeros((rows, 1), jnp.float32)
        image_dir = jnp.zeros(images.shape, jnp.float32)
        text_dir = jnp.zeros(texts.shape, jnp.float32)
        visits = [(text_group, image_group, True)] + [
            (t, i, False) for t, i in zip(text_blocks, image_blocks)]
        for text_block, image_block, diagonal in visits:
            image_dir, loss_total = visit(image_emb, text_block, image_dir, loss_total,
                                          params, offset, diagonal, True)
            text_dir, unused = visit(text_emb, image_block, text_dir, unused,
                                     params, offset, diagonal, False)
        loss_total = loss_total[:, 0]
        window = STEPS * n_pair * rows
        row_loss = loss_total / window
        grad_images = tangent(image_unit, image_inverse, image_dir)
        grad_texts = tangent(text_unit, text_inverse, text_dir)
        return (row_loss, grad_images, grad_texts)

    return body


def solution(mesh):
    in_specs = (P(("blk", "pair"), None), P(("blk", "pair"), None), P(), P())
    out_specs = (P(("blk", "pair")), P(("blk", "pair"), None), P(("blk", "pair"), None))
    return jax.shard_map(make_body(mesh), mesh=mesh, in_specs=in_specs, out_specs=out_specs, check_vma=False)
```
